128 devices in a mesh: clu: 8 (over y, x_hi), mem: 16 (over x_lo, z, core).
Axes of the slice: x: 4 (x_hi: 2, x_lo: 2; x = x_hi * 2 + x_lo), y: 4, z: 4, core: 2. Of those that a mesh axis runs over, the one named last changes fastest.
Arguments:
- embeddings: bfloat16 [131072, 768], P(('clu', 'mem'))
- block_order: int32 [8, 128], P('clu'), may hold values from 0 to 7, as said below
Outputs:
- weight: float32 [131072], P(('clu', 'mem'))
The draws below stay inside these ranges and needn't reach their ends.
Inputs may be any that keep to these rules, and one draw needn't show every extreme that they name: `block_order`: each aligned run of 8 entries is a permutation of 0 to 7.
All inputs are finite; a program needn't handle non-finite values.
Results may differ from the reference program's by a relative error of at most 0.0029.
Values may be sent and summed in bfloat16 or wider, within the bound.
No kernel may reach another device: no remote copies, remote signals or barrier semaphores. Data moves between devices by JAX's collectives and lax.ppermute only.
A program may use at most 64 MiB of HBM per device.

```python
import math
import jax
import jax.numpy as jnp
from jax import lax

D = 768
BLK = 128
BPD = 8
GBLK = 128
GROUPS = 8
ROWS = 131072
N_CLU = 8
N_MEM = 16


def draw_embeddings(key, part):
    centers_count = max(GBLK * BLK // 32, 2)
    supers_count = 8
    group_rows = GBLK * BLK
    key_label = jax.random.fold_in(key, 31)
    key_jitter = jax.random.fold_in(key, 32)
    key_noise = jax.random.fold_in(key, 33)
    key_subsq = jax.random.fold_in(key, 34)
    key_center = jax.random.fold_in(key, 35)
    key_parent = jax.random.fold_in(key, 36)
    key_supsq = jax.random.fold_in(key, 37)
    key_super = jax.random.fold_in(key, 38)
    key_common = jax.random.fold_in(key, 39)
    key_axes = jax.random.fold_in(key, 40)
    labels = jax.random.randint(key_label, (ROWS,), 0, centers_count)
    parents = jax.random.randint(key_parent, (centers_count,), 0, supers_count)
    position = jnp.arange(ROWS, dtype=jnp.float32) / ROWS
    jitter = jax.random.uniform(key_jitter, (ROWS,), jnp.float32)
    spread = 0.6 * position + 0.4 * jitter
    sigma_sq = 0.3 * jnp.power(8.0, spread)
    noise = jax.random.normal(key_noise, (ROWS, D), jnp.float32)
    center_noise = jax.random.normal(key_center, (centers_count, D), jnp.float32)
    super_noise = jax.random.normal(key_super, (supers_count, D), jnp.float32)
    common_noise = jax.random.normal(key_common, (GROUPS, D), jnp.float32)
    scale_low = 0.4
    scale_high = 1.6
    sub_low = 2.0
    sub_high = 8.0
    super_low = 1.0
    super_high = 6.0
    common_sq = 6.0
    scale_mean = (scale_high * scale_high - scale_low * scale_low) / (2.0 * math.log(scale_high / scale_low))
    axis_log = jax.random.uniform(key_axes, (D,), jnp.float32, math.log(scale_low), math.log(scale_high))
    axis_scale = jnp.exp(axis_log) / math.sqrt(scale_mean)
    root_width = jnp.sqrt(jnp.float32(D))
    sub_sq = jnp.exp(jax.random.uniform(key_subsq, (centers_count,), jnp.float32, math.log(sub_low), math.log(sub_high)))
    super_sq = jnp.exp(jax.random.uniform(key_supsq, (supers_count,), jnp.float32, math.log(super_low), math.log(super_high)))
    centers = center_noise * jnp.sqrt(sub_sq)[:, None] * axis_scale[None, :] / root_width
    supers = super_noise * jnp.sqrt(super_sq)[:, None] * axis_scale[None, :] / root_width
    commons = common_noise * math.sqrt(common_sq) * axis_scale[None, :] / root_width
    values = centers[labels] + supers[parents[labels]] + jnp.sqrt(sigma_sq)[:, None] * noise / root_width
    values = values.reshape(GROUPS, group_rows, D) + commons[:, None, :]
    return values.reshape(ROWS, D).astype(jnp.bfloat16)


def draw_block_order(key, part):
    runs = GROUPS * GBLK // BPD
    run_keys = jax.random.split(jax.random.fold_in(key, 21), runs)
    orders = jax.vmap(lambda one_key: jax.random.permutation(one_key, BPD))(run_keys)
    return orders.reshape(GROUPS, GBLK).astype(jnp.int32)


def setup_inputs(seed: int = 0) -> dict:
    splits = jax.random.split(jax.random.key(seed), 3)
    return {
        "embeddings": draw_embeddings(jax.random.fold_in(splits[2], 71), 0),
        "block_order": draw_block_order(jax.random.fold_in(splits[2], 71), 0),
    }


def class_table(count):
    spots = jnp.arange(count, dtype=jnp.int32)
    levels = count.bit_length() - 1
    classes = jnp.zeros((count,), jnp.int32)
    for level in range(1, levels + 1):
        classes = classes + (spots >= count - (count >> level)).astype(jnp.int32)
    return classes


def group_density(group_rows, group_ids):
    row_ids = jnp.repeat(group_ids, BLK)
    norms = jnp.sum(jnp.square(group_rows.astype(jnp.float32)), axis=1)
    block_len = BPD * BLK
    block_count = group_rows.shape[0] // block_len

    def one_block(index):
        start = (index * block_len).astype(jnp.int32)
        block = lax.dynamic_slice_in_dim(group_rows, start, block_len, 0)
        block_ids = lax.dynamic_slice_in_dim(row_ids, start, block_len, 0)
        block_norms = lax.dynamic_slice_in_dim(norms, start, block_len, 0)
        products = jnp.dot(block, group_rows.T, preferred_element_type=jnp.float32)
        distance = block_norms[:, None] + norms[None, :] - 2.0 * products
        kernel = jnp.where(block_ids[:, None] == row_ids[None, :], jnp.exp(-0.5 * distance), jnp.float32(0.0))
        return jnp.sum(kernel, axis=1)

    return lax.map(one_block, jnp.arange(block_count, dtype=jnp.int32)).reshape(-1)


def reference(embeddings, block_order):
    orders = block_order.reshape(N_CLU, N_MEM, BPD)
    classes = class_table(BPD)
    locals_range = jnp.arange(BPD, dtype=jnp.int32)
    matches = (orders[:, :, :, None] == locals_range[None, None, None, :]).astype(jnp.int32)
    local_class = jnp.sum(matches * classes[None, None, :, None], axis=2)
    group_ids = local_class.reshape(N_CLU, GBLK)
    grouped = embeddings.reshape(N_CLU, -1, D)
    density = lax.map(lambda pair: group_density(pair[0], pair[1]), (grouped, group_ids))
    inverse = 1.0 / density
    weight = inverse * (jnp.float32(ROWS) / jnp.sum(inverse))
    return weight.reshape(-1)
```

```python
import jax
import jax.numpy as jnp
from jax import lax
from jax.sharding import PartitionSpec as P

BLK = 128


def squared(values):
    return jnp.sum(jnp.square(values.astype(jnp.float32)), axis=1)


def class_table(count):
    spots = jnp.arange(count, dtype=jnp.int32)
    levels = count.bit_length() - 1
    classes = jnp.zeros((count,), jnp.int32)
    for level in range(1, levels + 1):
        classes = classes + (spots >= count - (count >> level)).astype(jnp.int32)
    return classes


def class_spans(count):
    spans = []
    start = 0
    width = count // 2
    while start < count:
        end = min(start + max(width, 1), count)
        spans.append((start, end))
        start = end
        width //= 2
    return spans


def pieces_of(spans, most):
    pieces = []
    for index, (start, end) in enumerate(spans):
        while start < end:
            stop = min(start + most, end)
            pieces.append((index, start, stop))
            start = stop
    return pieces


def tree_total(value, axis, size):
    stride = 1
    while stride < size:
        if stride * 4 <= size:
            def swap(k):
                return lax.ppermute(value, axis, [(i, i ^ k) for i in range(size)])
            one, two, three = swap(stride), swap(2 * stride), swap(3 * stride)
            value = (value + one) + (two + three)
            stride *= 4
        else:
            value = value + lax.ppermute(value, axis, [(i, i ^ stride) for i in range(size)])
            stride *= 2
    return value


def shards(embeddings, block_order):
    row_count, width = embeddings.shape
    member_count = lax.axis_size("mem")
    position = lax.axis_index("mem")
    per_device = row_count // BLK
    order = lax.dynamic_slice_in_dim(block_order[0], position * per_device, per_device)
    blocks = embeddings.reshape(per_device, BLK, width)
    ordered = jnp.take(blocks, order, axis=0)
    spans = class_spans(per_device)
    pieces = pieces_of(spans, max(per_device // 4, 1))

    own = [ordered[start:end].reshape(-1, width) for start, end in spans]
    own_norms = [squared(rows) for rows in own]
    density = [jnp.zeros((rows.shape[0],), jnp.float32) for rows in own]
    for index, start, stop in pieces:
        other = lax.all_gather(ordered[start:stop].reshape(-1, width), "mem", axis=0, tiled=True)
        products = lax.dot_general(
            own[index], other, (((1,), (1,)), ((), ())), preferred_element_type=jnp.float32
        )
        distance = own_norms[index][:, None] + squared(other)[None, :] - 2.0 * products
        density[index] = density[index] + jnp.sum(jnp.exp(-0.5 * distance), axis=1)

    inverse = 1.0 / jnp.concatenate(density).reshape(per_device, BLK)
    total = tree_total(jnp.sum(inverse), "mem", member_count)
    total = tree_total(total, "clu", lax.axis_size("clu"))
    everything = jnp.float32(row_count * lax.axis_size("clu") * member_count)
    weight = inverse * (everything / total)
    spots = jnp.arange(per_device, dtype=jnp.int32)
    back = jnp.sum(
        jnp.where(order[None, :] == spots[:, None], spots[None, :], 0), axis=1
    )
    return jnp.take(weight, back, axis=0).reshape(-1)


def solution(mesh):
    placed = (P(("clu", "mem"), None), P("clu", None))
    return jax.shard_map(
        shards, mesh=mesh, in_specs=placed, out_specs=P(("clu", "mem")), check_vma=False
    )
```

```python
import itertools

import jax
import jax.numpy as jnp
from jax import lax
from jax.sharding import PartitionSpec as P

BLK = 128


def squared(values):
    return jnp.sum(jnp.square(values.astype(jnp.float32)), axis=1)


def class_spans(count):
    spans = []
    start = 0
    width = count // 2
    while start < count:
        end = min(start + max(width, 1), count)
        spans.append((start, end))
        start = end
        width //= 2
    return spans


def member_ring(count):
    if count != 16:
        return list(range(count))
    chips = [(0, 0), (0, 1), (0, 2), (0, 3), (1, 3), (1, 2), (1, 1), (1, 0)]
    return [x * 8 + z * 2 + core for x, z in chips for core in (0, 1)]


def cover(count):
    best = None
    half = count // 2
    for size in range(2, count + 1):
        for rest in itertools.combinations(range(1, count), size - 1):
            offsets = (0,) + rest
            kinds = set()
            for a, b in itertools.combinations(offsets, 2):
                step = (b - a) % count
                kinds.add(min(step, count - step))
            if kinds >= set(range(1, half + 1)):
                cost = sum(min(d, count - d) for d in rest)
                if best is None or cost < best[0]:
                    best = (cost, offsets)
        if best is not None:
            return best[1]
    return tuple(range(count))


def plan(count):
    offsets = cover(count)
    pairs = []
    for step in range(1, count // 2 + 1):
        for a, b in itertools.permutations(offsets, 2):
            if (b - a) % count == step:
                pairs.append((a, b, 2 * step != count))
                break
    return offsets, pairs


def tree_total(value, axis, size):
    stride = 1
    while stride < size:
        value = value + lax.ppermute(value, axis, [(i, i ^ stride) for i in range(size)])
        stride *= 2
    return value


def kernel_sums(left, right, left_norms, right_norms, both):
    products = lax.dot_general(
        left, right, (((1,), (1,)), ((), ())), preferred_element_type=jnp.float32
    )
    distance = left_norms[:, None] + right_norms[None, :] - 2.0 * products
    kernel = jnp.exp(-0.5 * distance)
    rows = jnp.sum(kernel, axis=1)
    cols = jnp.sum(kernel, axis=0) if both else None
    return rows, cols


def shards(embeddings, block_order):
    row_count, width = embeddings.shape
    member_count = lax.axis_size("mem")
    position = lax.axis_index("mem")
    per_device = row_count // BLK
    order = lax.dynamic_slice_in_dim(block_order[0], position * per_device, per_device)
    blocks = embeddings.reshape(per_device, BLK, width)
    ordered = jnp.take(blocks, order, axis=0).reshape(row_count, width)
    spans = [(start * BLK, end * BLK) for start, end in class_spans(per_device)]

    ring = member_ring(member_count)
    offsets, pairs = plan(member_count)

    def fetch(value, offset):
        return lax.ppermute(
            value,
            "mem",
            [(ring[(r + offset) % member_count], ring[r]) for r in range(member_count)],
        )

    def give_back(value, offset):
        return lax.ppermute(
            value,
            "mem",
            [(ring[r], ring[(r + offset) % member_count]) for r in range(member_count)],
        )

    held = {0: ordered}
    for offset in offsets[1:]:
        held[offset] = fetch(ordered, offset)
    norms = {offset: squared(rows) for offset, rows in held.items()}
    partial = {offset: [None] * len(spans) for offset in offsets}

    def add(offset, index, value):
        slot = partial[offset]
        slot[index] = value if slot[index] is None else slot[index] + value

    for index, (start, end) in enumerate(spans):
        own = held[0][start:end]
        own_norms = norms[0][start:end]
        rows, _ = kernel_sums(own, own, own_norms, own_norms, False)
        add(0, index, rows)
        for a, b, both in pairs:
            rows, cols = kernel_sums(
                held[a][start:end], held[b][start:end],
                norms[a][start:end], norms[b][start:end], both,
            )
            add(a, index, rows)
            if both:
                add(b, index, cols)

    gathered = {}
    for offset in offsets:
        parts = [
            value if value is not None else jnp.zeros((end - start,), jnp.float32)
            for value, (start, end) in zip(partial[offset], spans)
        ]
        gathered[offset] = jnp.concatenate(parts)
    density = gathered[0]
    for offset in offsets[1:]:
        density = density + give_back(gathered[offset], offset)

    inverse = 1.0 / density.reshape(per_device, BLK)
    total = tree_total(jnp.sum(inverse), "mem", member_count)
    total = tree_total(total, "clu", lax.axis_size("clu"))
    everything = jnp.float32(row_count * lax.axis_size("clu") * member_count)
    weight = inverse * (everything / total)
    spots = jnp.arange(per_device, dtype=jnp.int32)
    back = jnp.sum(
        jnp.where(order[None, :] == spots[:, None], spots[None, :], 0), axis=1
    )
    return jnp.take(weight, back, axis=0).reshape(-1)


def solution(mesh):
    placed = (P(("clu", "mem"), None), P("clu", None))
    return jax.shard_map(
        shards, mesh=mesh, in_specs=placed, out_specs=P(("clu", "mem")), check_vma=False
    )
```

```python
import itertools

import jax
import jax.numpy as jnp
from jax import lax
from jax.sharding import PartitionSpec as P

BLK = 128


def squared(values):
    return jnp.sum(jnp.square(values.astype(jnp.float32)), axis=1)


def class_spans(count):
    spans = []
    start = 0
    width = count // 2
    while start < count:
        end = min(start + max(width, 1), count)
        spans.append((start, end))
        start = end
        width //= 2
    return spans


def member_ring(count):
    if count != 16:
        return list(range(count))
    chips = [(0, 0), (0, 1), (0, 2), (0, 3), (1, 3), (1, 2), (1, 1), (1, 0)]
    return [x * 8 + z * 2 + core for core in (0, 1) for x, z in chips]


def cover(count):
    if count == 16:
        return (0, 1, 5, 8, 15)
    best = None
    half = count // 2
    for size in range(2, count + 1):
        for rest in itertools.combinations(range(1, count), size - 1):
            offsets = (0,) + rest
            kinds = set()
            for a, b in itertools.combinations(offsets, 2):
                step = (b - a) % count
                kinds.add(min(step, count - step))
            if kinds >= set(range(1, half + 1)):
                cost = sum(min(d, count - d) for d in rest)
                if best is None or cost < best[0]:
                    best = (cost, offsets)
        if best is not None:
            return best[1]
    return tuple(range(count))


def plan(count):
    offsets = cover(count)
    pairs = []
    for step in range(1, count // 2 + 1):
        for a, b in itertools.permutations(offsets, 2):
            if (b - a) % count == step:
                pairs.append((a, b, 2 * step != count))
                break
    return offsets, pairs


def grand_total(value, axes, size):
    spread = lax.all_to_all(jnp.broadcast_to(value, (size, 1)), axes, 0, 0, tiled=True)
    return jnp.sum(spread)


def kernel_sums(left, right, left_norms, right_norms, both):
    products = lax.dot_general(
        left, right, (((1,), (1,)), ((), ())), preferred_element_type=jnp.float32
    )
    distance = left_norms[:, None] + right_norms[None, :] - 2.0 * products
    kernel = jnp.exp(-0.5 * distance)
    rows = jnp.sum(kernel, axis=1)
    cols = jnp.sum(kernel, axis=0) if both else None
    return rows, cols


def shards(embeddings, block_order):
    row_count, width = embeddings.shape
    member_count = lax.axis_size("mem")
    position = lax.axis_index("mem")
    per_device = row_count // BLK
    order = lax.dynamic_slice_in_dim(block_order[0], position * per_device, per_device)
    blocks = embeddings.reshape(per_device, BLK, width)
    ordered = jnp.take(blocks, order, axis=0).reshape(row_count, width)
    spans = [(start * BLK, end * BLK) for start, end in class_spans(per_device)]

    ring = member_ring(member_count)
    offsets, pairs = plan(member_count)

    def fetch(value, offset):
        return lax.ppermute(
            value,
            "mem",
            [(ring[(r + offset) % member_count], ring[r]) for r in range(member_count)],
        )

    def give_back(value, offset):
        return lax.ppermute(
            value,
            "mem",
            [(ring[r], ring[(r + offset) % member_count]) for r in range(member_count)],
        )

    held = {0: ordered}
    for offset in offsets[1:]:
        held[offset] = fetch(ordered, offset)
    norms = {offset: squared(rows) for offset, rows in held.items()}
    partial = {offset: [None] * len(spans) for offset in offsets}

    def add(offset, index, value):
        slot = partial[offset]
        slot[index] = value if slot[index] is None else slot[index] + value

    for index, (start, end) in enumerate(spans):
        own = held[0][start:end]
        own_norms = norms[0][start:end]
        rows, _ = kernel_sums(own, own, own_norms, own_norms, False)
        add(0, index, rows)
        for a, b, both in pairs:
            rows, cols = kernel_sums(
                held[a][start:end], held[b][start:end],
                norms[a][start:end], norms[b][start:end], both,
            )
            add(a, index, rows)
            if both:
                add(b, index, cols)

    gathered = {}
    for offset in offsets:
        parts = [
            value if value is not None else jnp.zeros((end - start,), jnp.float32)
            for value, (start, end) in zip(partial[offset], spans)
        ]
        gathered[offset] = jnp.concatenate(parts)
    density = gathered[0]
    for offset in offsets[1:]:
        density = density + give_back(gathered[offset], offset)

    inverse = 1.0 / density.reshape(per_device, BLK)
    total = grand_total(jnp.sum(inverse), ("clu", "mem"), lax.axis_size("clu") * member_count)
    everything = jnp.float32(row_count * lax.axis_size("clu") * member_count)
    weight = inverse * (everything / total)
    spots = jnp.arange(per_device, dtype=jnp.int32)
    back = jnp.sum(
        jnp.where(order[None, :] == spots[:, None], spots[None, :], 0), axis=1
    )
    return jnp.take(weight, back, axis=0).reshape(-1)


def solution(mesh):
    placed = (P(("clu", "mem"), None), P("clu", None))
    return jax.shard_map(
        shards, mesh=mesh, in_specs=placed, out_specs=P(("clu", "mem")), check_vma=False
    )
```

```python
import itertools

import jax
import jax.numpy as jnp
from jax import lax
from jax.sharding import PartitionSpec as P


BLK = 128


def squared(values):
    return jnp.sum(jnp.square(values.astype(jnp.float32)), axis=1)


def class_spans(count):
    spans = []
    start = 0
    width = count // 2
    while start < count:
        end = min(start + max(width, 1), count)
        spans.append((start, end))
        start = end
        width //= 2
    return spans


def member_ring(count):
    if count != 16:
        return list(range(count))
    chips = [(0, 0), (0, 1), (0, 2), (0, 3), (1, 3), (1, 2), (1, 1), (1, 0)]
    return [x * 8 + z * 2 + core for core in (0, 1) for x, z in chips]


def cover(count):
    if count == 16:
        return (0, 1, 5, 8, 15)
    best = None
    half = count // 2
    for size in range(2, count + 1):
        for rest in itertools.combinations(range(1, count), size - 1):
            offsets = (0,) + rest
            kinds = set()
            for a, b in itertools.combinations(offsets, 2):
                step = (b - a) % count
                kinds.add(min(step, count - step))
            if kinds >= set(range(1, half + 1)):
                cost = sum(min(d, count - d) for d in rest)
                if best is None or cost < best[0]:
                    best = (cost, offsets)
        if best is not None:
            return best[1]
    return tuple(range(count))


def plan(count):
    offsets = cover(count)
    pairs = []
    for step in range(1, count // 2 + 1):
        for a, b in itertools.permutations(offsets, 2):
            if (b - a) % count == step:
                pairs.append((a, b, 2 * step != count))
                break
    return offsets, pairs


def grand_total(value, axes, size):
    spread = lax.all_to_all(jnp.broadcast_to(value, (size, 1)), axes, 0, 0, tiled=True)
    return jnp.sum(spread)


def kernel_sums(left, right, left_norms, right_norms, both):
    products = lax.dot_general(
        left, right, (((1,), (1,)), ((), ())), preferred_element_type=jnp.float32
    )
    distance = left_norms[:, None] + right_norms[None, :] - 2.0 * products
    kernel = jnp.exp(-0.5 * distance)
    rows = jnp.sum(kernel, axis=1)
    cols = jnp.sum(kernel, axis=0) if both else None
    return rows, cols


def shards(embeddings, block_order):
    row_count, width = embeddings.shape
    member_count = lax.axis_size("mem")
    position = lax.axis_index("mem")
    per_device = row_count // BLK
    order = lax.dynamic_slice_in_dim(block_order[0], position * per_device, per_device)
    blocks = embeddings.reshape(per_device, BLK, width)
    ordered = jnp.take(blocks, order, axis=0).reshape(row_count, width)
    spans = [(start * BLK, end * BLK) for start, end in class_spans(per_device)]

    ring = member_ring(member_count)
    offsets, pairs = plan(member_count)

    def fetch(value, offset):
        return lax.ppermute(
            value,
            "mem",
            [(ring[(r + offset) % member_count], ring[r]) for r in range(member_count)],
        )

    def give_back(value, offset):
        return lax.ppermute(
            value,
            "mem",
            [(ring[r], ring[(r + offset) % member_count]) for r in range(member_count)],
        )

    late = offsets[-1]
    held = {0: ordered}
    for offset in [late] + [o for o in offsets[1:] if o != late]:
        held[offset] = fetch(ordered, offset)
    norms = {}
    partial = {offset: [None] * len(spans) for offset in offsets}

    def add(offset, index, value):
        slot = partial[offset]
        slot[index] = value if slot[index] is None else slot[index] + value

    def blocks(chosen):
        for offset in {o for a, b, _ in chosen for o in (a, b)} | {0}:
            if offset not in norms:
                norms[offset] = squared(held[offset])
        for index, (start, end) in enumerate(spans):
            for a, b, both in chosen:
                rows, cols = kernel_sums(
                    held[a][start:end], held[b][start:end],
                    norms[a][start:end], norms[b][start:end], both,
                )
                add(a, index, rows)
                if both:
                    add(b, index, cols)

    blocks([(0, 0, False)] + [p for p in pairs if late not in p[:2]])
    blocks([p for p in pairs if late in p[:2]])

    gathered = {}
    for offset in offsets:
        parts = [
            value if value is not None else jnp.zeros((end - start,), jnp.float32)
            for value, (start, end) in zip(partial[offset], spans)
        ]
        gathered[offset] = jnp.concatenate(parts)
    density = gathered[0]
    for offset in offsets[1:]:
        density = density + give_back(gathered[offset], offset)

    inverse = 1.0 / density.reshape(per_device, BLK)
    total = grand_total(jnp.sum(inverse), ("clu", "mem"), lax.axis_size("clu") * member_count)
    everything = jnp.float32(row_count * lax.axis_size("clu") * member_count)
    weight = inverse * (everything / total)
    spots = jnp.arange(per_device, dtype=jnp.int32)
    back = jnp.sum(
        jnp.where(order[None, :] == spots[:, None], spots[None, :], 0), axis=1
    )
    return jnp.take(weight, back, axis=0).reshape(-1)


def solution(mesh):
    placed = (P(("clu", "mem"), None), P("clu", None))
    return jax.shard_map(
        shards, mesh=mesh, in_specs=placed, out_specs=P(("clu", "mem")), check_vma=False
    )
```

```python
import itertools

import jax
import jax.numpy as jnp
from jax import lax
from jax.sharding import PartitionSpec as P


BLK = 128


def squared(values):
    return jnp.sum(jnp.square(values.astype(jnp.float32)), axis=1)


def class_spans(count):
    spans = []
    start = 0
    width = count // 2
    while start < count:
        end = min(start + max(width, 1), count)
        spans.append((start, end))
        start = end
        width //= 2
    return spans


def member_ring(count):
    if count != 16:
        return list(range(count))
    chips = [(0, 0), (0, 1), (0, 2), (0, 3), (1, 3), (1, 2), (1, 1), (1, 0)]
    return [x * 8 + z * 2 + core for core in (0, 1) for x, z in chips]


def cover(count):
    if count == 16:
        return (0, 1, 5, 8, 15)
    best = None
    half = count // 2
    for size in range(2, count + 1):
        for rest in itertools.combinations(range(1, count), size - 1):
            offsets = (0,) + rest
            kinds = set()
            for a, b in itertools.combinations(offsets, 2):
                step = (b - a) % count
                kinds.add(min(step, count - step))
            if kinds >= set(range(1, half + 1)):
                cost = sum(min(d, count - d) for d in rest)
                if best is None or cost < best[0]:
                    best = (cost, offsets)
        if best is not None:
            return best[1]
    return tuple(range(count))


def plan(count):
    offsets = cover(count)
    pairs = []
    for step in range(1, count // 2 + 1):
        for a, b in itertools.permutations(offsets, 2):
            if (b - a) % count == step:
                pairs.append((a, b, 2 * step != count))
                break
    return offsets, pairs


def grand_total(value, axes, size):
    spread = lax.all_to_all(jnp.broadcast_to(value, (size, 1)), axes, 0, 0, tiled=True)
    return jnp.sum(spread)


def kernel_sums(left, right, left_norms, right_norms, both):
    products = lax.dot_general(
        left, right, (((1,), (1,)), ((), ())), preferred_element_type=jnp.float32
    )
    distance = left_norms[:, None] + right_norms[None, :] - 2.0 * products
    kernel = jnp.exp(-0.5 * distance)
    rows = jnp.sum(kernel, axis=1)
    cols = jnp.sum(kernel, axis=0) if both else None
    return rows, cols


def shards(embeddings, block_order):
    row_count, width = embeddings.shape
    member_count = lax.axis_size("mem")
    position = lax.axis_index("mem")
    per_device = row_count // BLK
    order = lax.dynamic_slice_in_dim(block_order[0], position * per_device, per_device)
    blocks = embeddings.reshape(per_device, BLK, width)
    ordered = jnp.take(blocks, order, axis=0).reshape(row_count, width)
    spans = [(start * BLK, end * BLK) for start, end in class_spans(per_device)]

    ring = member_ring(member_count)
    offsets, pairs = plan(member_count)

    def fetch(value, offset):
        return lax.ppermute(
            value,
            "mem",
            [(ring[(r + offset) % member_count], ring[r]) for r in range(member_count)],
        )

    def give_back(value, offset):
        return lax.ppermute(
            value,
            "mem",
            [(ring[r], ring[(r + offset) % member_count]) for r in range(member_count)],
        )

    late = offsets[-1]
    held = {0: ordered}
    for offset in offsets[1:]:
        held[offset] = fetch(ordered, offset)
    norms = {}
    partial = {offset: [None] * len(spans) for offset in offsets}

    def add(offset, index, value):
        slot = partial[offset]
        slot[index] = value if slot[index] is None else slot[index] + value

    def blocks(chosen):
        for offset in {o for a, b, _ in chosen for o in (a, b)} | {0}:
            if offset not in norms:
                norms[offset] = squared(held[offset])
        for index, (start, end) in enumerate(spans):
            for a, b, both in chosen:
                rows, cols = kernel_sums(
                    held[a][start:end], held[b][start:end],
                    norms[a][start:end], norms[b][start:end], both,
                )
                add(a, index, rows)
                if both:
                    add(b, index, cols)

    late_pairs = [p for p in pairs if late in p[:2]]
    blocks([(0, 0, False)] + [p for p in pairs if late not in p[:2]])
    partial = lax.optimization_barrier(partial)
    blocks(late_pairs)

    def joined(offset):
        parts = [
            value if value is not None else jnp.zeros((end - start,), jnp.float32)
            for value, (start, end) in zip(partial[offset], spans)
        ]
        return jnp.concatenate(parts)

    density = joined(0)
    for offset in offsets[1:]:
        density = density + give_back(joined(offset), offset)

    inverse = 1.0 / density.reshape(per_device, BLK)
    total = grand_total(jnp.sum(inverse), ("clu", "mem"), lax.axis_size("clu") * member_count)
    everything = jnp.float32(row_count * lax.axis_size("clu") * member_count)
    weight = inverse * (everything / total)
    spots = jnp.arange(per_device, dtype=jnp.int32)
    back = jnp.sum(
        jnp.where(order[None, :] == spots[:, None], spots[None, :], 0), axis=1
    )
    return jnp.take(weight, back, axis=0).reshape(-1)


def solution(mesh):
    placed = (P(("clu", "mem"), None), P("clu", None))
    return jax.shard_map(
        shards, mesh=mesh, in_specs=placed, out_specs=P(("clu", "mem")), check_vma=False
    )
```

```python
import itertools

import jax
import jax.numpy as jnp
from jax import lax
from jax.sharding import PartitionSpec as P


BLK = 128


def squared(values):
    return jnp.sum(jnp.square(values.astype(jnp.float32)), axis=1)


def class_spans(count):
    spans = []
    start = 0
    width = count // 2
    while start < count:
        end = min(start + max(width, 1), count)
        spans.append((start, end))
        start = end
        width //= 2
    return spans


def member_ring(count):
    if count != 16:
        return list(range(count))
    chips = [(0, 0), (0, 1), (0, 2), (0, 3), (1, 3), (1, 2), (1, 1), (1, 0)]
    return [x * 8 + z * 2 + core for core in (0, 1) for x, z in chips]


def cover(count):
    if count == 16:
        return (0, 1, 5, 8, 15)
    best = None
    half = count // 2
    for size in range(2, count + 1):
        for rest in itertools.combinations(range(1, count), size - 1):
            offsets = (0,) + rest
            kinds = set()
            for a, b in itertools.combinations(offsets, 2):
                step = (b - a) % count
                kinds.add(min(step, count - step))
            if kinds >= set(range(1, half + 1)):
                cost = sum(min(d, count - d) for d in rest)
                if best is None or cost < best[0]:
                    best = (cost, offsets)
        if best is not None:
            return best[1]
    return tuple(range(count))


def plan(count):
    offsets = cover(count)
    pairs = []
    for step in range(1, count // 2 + 1):
        for a, b in itertools.permutations(offsets, 2):
            if (b - a) % count == step:
                pairs.append((a, b, 2 * step != count))
                break
    return offsets, pairs


def grand_total(value, axes, size):
    spread = lax.all_to_all(jnp.broadcast_to(value, (size,)), axes, 0, 0, tiled=True)
    return jnp.sum(spread)


def kernel_sums(left, right, left_norms, right_norms, both):
    products = lax.dot_general(
        left, right, (((1,), (1,)), ((), ())), preferred_element_type=jnp.float32
    )
    distance = left_norms[:, None] + right_norms[None, :] - 2.0 * products
    kernel = jnp.exp(-0.5 * distance)
    rows = jnp.sum(kernel, axis=1)
    cols = jnp.sum(kernel, axis=0) if both else None
    return rows, cols


def shards(embeddings, block_order):
    row_count, width = embeddings.shape
    member_count = lax.axis_size("mem")
    position = lax.axis_index("mem")
    per_device = row_count // BLK
    order = lax.dynamic_slice_in_dim(block_order[0], position * per_device, per_device)
    blocks = embeddings.reshape(per_device, BLK, width)
    ordered = jnp.take(blocks, order, axis=0).reshape(row_count, width)
    spans = [(start * BLK, end * BLK) for start, end in class_spans(per_device)]

    ring = member_ring(member_count)
    offsets, pairs = plan(member_count)

    def fetch(value, offset):
        return lax.ppermute(
            value,
            "mem",
            [(ring[(r + offset) % member_count], ring[r]) for r in range(member_count)],
        )

    def give_back(value, offset):
        return lax.ppermute(
            value,
            "mem",
            [(ring[r], ring[(r + offset) % member_count]) for r in range(member_count)],
        )

    late = offsets[-1]
    held = {0: ordered}
    for offset in offsets[1:]:
        held[offset] = fetch(ordered, offset)
    norms = {}
    partial = {offset: [None] * len(spans) for offset in offsets}

    def add(offset, index, value):
        slot = partial[offset]
        slot[index] = value if slot[index] is None else slot[index] + value

    def blocks(chosen):
        for offset in {o for a, b, _ in chosen for o in (a, b)} | {0}:
            if offset not in norms:
                norms[offset] = squared(held[offset])
        for index, (start, end) in enumerate(spans):
            for a, b, both in chosen:
                rows, cols = kernel_sums(
                    held[a][start:end], held[b][start:end],
                    norms[a][start:end], norms[b][start:end], both,
                )
                add(a, index, rows)
                if both:
                    add(b, index, cols)

    late_pairs = [p for p in pairs if late in p[:2]]
    blocks([(0, 0, False)] + [p for p in pairs if late not in p[:2]])
    partial = lax.optimization_barrier(partial)
    blocks(late_pairs)

    def joined(offset):
        parts = [
            value if value is not None else jnp.zeros((end - start,), jnp.float32)
            for value, (start, end) in zip(partial[offset], spans)
        ]
        return jnp.concatenate(parts)

    touched = {o for a, b, both in late_pairs for o in ((a, b) if both else (a,))}
    density = joined(0)
    for offset in [o for o in offsets[1:] if o not in touched]:
        density = density + give_back(joined(offset), offset)
    for offset in [o for o in offsets[1:] if o in touched]:
        density = density + give_back(joined(offset), offset)

    inverse = 1.0 / density.reshape(per_device, BLK)
    total = grand_total(jnp.sum(inverse), ("clu", "mem"), lax.axis_size("clu") * member_count)
    everything = jnp.float32(row_count * lax.axis_size("clu") * member_count)
    weight = inverse * (everything / total)
    spots = jnp.arange(per_device, dtype=jnp.int32)
    back = jnp.sum(
        jnp.where(order[None, :] == spots[:, None], spots[None, :], 0), axis=1
    )
    return jnp.take(weight, back, axis=0).reshape(-1)


def solution(mesh):
    placed = (P(("clu", "mem"), None), P("clu", None))
    return jax.shard_map(
        shards, mesh=mesh, in_specs=placed, out_specs=P(("clu", "mem")), check_vma=False
    )
```

```python
import itertools

import jax
import jax.numpy as jnp
from jax import lax
from jax.sharding import PartitionSpec as P


BLK = 128


def squared(values):
    return jnp.sum(jnp.square(values.astype(jnp.float32)), axis=1)


def class_spans(count):
    spans = []
    start = 0
    width = count // 2
    while start < count:
        end = min(start + max(width, 1), count)
        spans.append((start, end))
        start = end
        width //= 2
    return spans


def member_ring(count):
    if count != 16:
        return list(range(count))
    chips = [(0, 0), (0, 1), (0, 2), (0, 3), (1, 3), (1, 2), (1, 1), (1, 0)]
    return [x * 8 + z * 2 + core for core in (0, 1) for x, z in chips]


def cover(count):
    if count == 16:
        return (0, 1, 5, 8, 15)
    best = None
    half = count // 2
    for size in range(2, count + 1):
        for rest in itertools.combinations(range(1, count), size - 1):
            offsets = (0,) + rest
            kinds = set()
            for a, b in itertools.combinations(offsets, 2):
                step = (b - a) % count
                kinds.add(min(step, count - step))
            if kinds >= set(range(1, half + 1)):
                cost = sum(min(d, count - d) for d in rest)
                if best is None or cost < best[0]:
                    best = (cost, offsets)
        if best is not None:
            return best[1]
    return tuple(range(count))


def plan(count):
    offsets = cover(count)
    pairs = []
    for step in range(1, count // 2 + 1):
        for a, b in itertools.permutations(offsets, 2):
            if (b - a) % count == step:
                pairs.append((a, b, 2 * step != count))
                break
    return offsets, pairs


def grand_total(value, axes, size):
    spread = lax.all_to_all(jnp.broadcast_to(value, (size,)), axes, 0, 0, tiled=True)
    return jnp.sum(spread)


def kernel_sums(left, right, left_norms, right_norms, both):
    products = lax.dot_general(
        left, right, (((1,), (1,)), ((), ())), preferred_element_type=jnp.float32
    )
    distance = left_norms[:, None] + right_norms[None, :] - 2.0 * products
    kernel = jnp.exp(-0.5 * distance)
    rows = jnp.sum(kernel, axis=1)
    cols = jnp.sum(kernel, axis=0) if both else None
    return rows, cols


def shards(embeddings, block_order):
    row_count, width = embeddings.shape
    member_count = lax.axis_size("mem")
    position = lax.axis_index("mem")
    per_device = row_count // BLK
    order = lax.dynamic_slice_in_dim(block_order[0], position * per_device, per_device)
    blocks = embeddings.reshape(per_device, BLK, width)
    ordered = jnp.take(blocks, order, axis=0).reshape(row_count, width)
    spans = [(start * BLK, end * BLK) for start, end in class_spans(per_device)]

    ring = member_ring(member_count)
    offsets, pairs = plan(member_count)

    def fetch(value, offset):
        return lax.ppermute(
            value,
            "mem",
            [(ring[(r + offset) % member_count], ring[r]) for r in range(member_count)],
        )

    def give_back(value, offset):
        return lax.ppermute(
            value,
            "mem",
            [(ring[r], ring[(r + offset) % member_count]) for r in range(member_count)],
        )

    late = offsets[-1]
    held = {0: ordered}
    for offset in offsets[1:]:
        held[offset] = fetch(ordered, offset)
    norms = {}
    partial = {offset: [None] * len(spans) for offset in offsets}

    def add(offset, index, value):
        slot = partial[offset]
        slot[index] = value if slot[index] is None else slot[index] + value

    def blocks(chosen):
        for offset in {o for a, b, _ in chosen for o in (a, b)} | {0}:
            if offset not in norms:
                norms[offset] = squared(held[offset])
        groups = {}
        for a, b, both in chosen:
            groups.setdefault((a, both), []).append(b)
        for index, (start, end) in enumerate(spans):
            for (a, both), others in groups.items():
                if not both:
                    for b in others:
                        rows, _ = kernel_sums(
                            held[a][start:end], held[b][start:end],
                            norms[a][start:end], norms[b][start:end], False,
                        )
                        add(a, index, rows)
                    continue
                rows, cols = kernel_sums(
                    held[a][start:end],
                    jnp.concatenate([held[b][start:end] for b in others]),
                    norms[a][start:end],
                    jnp.concatenate([norms[b][start:end] for b in others]),
                    True,
                )
                add(a, index, rows)
                for slot, b in enumerate(others):
                    add(b, index, cols[slot * (end - start):(slot + 1) * (end - start)])

    late_pairs = [p for p in pairs if late in p[:2]]
    blocks([(0, 0, False)] + [p for p in pairs if late not in p[:2]])
    partial = lax.optimization_barrier(partial)
    blocks(late_pairs)

    def joined(offset):
        parts = [
            value if value is not None else jnp.zeros((end - start,), jnp.float32)
            for value, (start, end) in zip(partial[offset], spans)
        ]
        return jnp.concatenate(parts)

    touched = {o for a, b, both in late_pairs for o in ((a, b) if both else (a,))}
    density = joined(0)
    for offset in [o for o in offsets[1:] if o not in touched]:
        density = density + give_back(joined(offset), offset)
    for offset in [o for o in offsets[1:] if o in touched]:
        density = density + give_back(joined(offset), offset)

    inverse = 1.0 / density.reshape(per_device, BLK)
    total = grand_total(jnp.sum(inverse), ("clu", "mem"), lax.axis_size("clu") * member_count)
    everything = jnp.float32(row_count * lax.axis_size("clu") * member_count)
    spots = jnp.arange(per_device, dtype=jnp.int32)
    back = jnp.sum(
        jnp.where(order[None, :] == spots[:, None], spots[None, :], 0), axis=1
    )
    stored = jnp.take(inverse, back, axis=0).reshape(-1)
    return stored * (everything / total)


def solution(mesh):
    placed = (P(("clu", "mem"), None), P("clu", None))
    return jax.shard_map(
        shards, mesh=mesh, in_specs=placed, out_specs=P(("clu", "mem")), check_vma=False
    )
```

```python
import itertools

import jax
import jax.numpy as jnp
from jax import lax
from jax.sharding import PartitionSpec as P


BLK = 128


def squared(values):
    return jnp.sum(jnp.square(values.astype(jnp.float32)), axis=1)


def class_spans(count):
    spans = []
    start = 0
    width = count // 2
    while start < count:
        end = min(start + max(width, 1), count)
        spans.append((start, end))
        start = end
        width //= 2
    return spans


def member_ring(count):
    if count != 16:
        return list(range(count))
    chips = [(0, 0), (0, 1), (0, 2), (0, 3), (1, 3), (1, 2), (1, 1), (1, 0)]
    return [x * 8 + z * 2 + core for core in (0, 1) for x, z in chips]


def cover(count):
    if count == 16:
        return (0, 1, 5, 8, 15)
    best = None
    half = count // 2
    for size in range(2, count + 1):
        for rest in itertools.combinations(range(1, count), size - 1):
            offsets = (0,) + rest
            kinds = set()
            for a, b in itertools.combinations(offsets, 2):
                step = (b - a) % count
                kinds.add(min(step, count - step))
            if kinds >= set(range(1, half + 1)):
                cost = sum(min(d, count - d) for d in rest)
                if best is None or cost < best[0]:
                    best = (cost, offsets)
        if best is not None:
            return best[1]
    return tuple(range(count))


def plan(count):
    offsets = cover(count)
    pairs = []
    for step in range(1, count // 2 + 1):
        for a, b in itertools.permutations(offsets, 2):
            if (b - a) % count == step:
                pairs.append((a, b, 2 * step != count))
                break
    return offsets, pairs


def grand_total(value, axes, size):
    spread = lax.all_to_all(jnp.broadcast_to(value, (size,)), axes, 0, 0, tiled=True)
    return jnp.sum(spread)


def kernel_sums(left, right, left_norms, right_norms, both):
    products = lax.dot_general(
        left, right, (((1,), (1,)), ((), ())), preferred_element_type=jnp.float32
    )
    distance = left_norms[:, None] + right_norms[None, :] - 2.0 * products
    kernel = jnp.exp(-0.5 * distance)
    rows = jnp.sum(kernel, axis=1)
    cols = jnp.sum(kernel, axis=0) if both else None
    return rows, cols


def shards(embeddings, block_order):
    row_count, width = embeddings.shape
    member_count = lax.axis_size("mem")
    position = lax.axis_index("mem")
    per_device = row_count // BLK
    order = lax.dynamic_slice_in_dim(block_order[0], position * per_device, per_device)
    blocks = embeddings.reshape(per_device, BLK, width)
    ordered = jnp.take(blocks, order, axis=0).reshape(row_count, width)
    spans = [(start * BLK, end * BLK) for start, end in class_spans(per_device)]

    ring = member_ring(member_count)
    offsets, pairs = plan(member_count)

    def fetch(value, offset):
        return lax.ppermute(
            value,
            "mem",
            [(ring[(r + offset) % member_count], ring[r]) for r in range(member_count)],
        )

    def give_back(value, offset):
        return lax.ppermute(
            value,
            "mem",
            [(ring[r], ring[(r + offset) % member_count]) for r in range(member_count)],
        )

    late = offsets[-1]
    first = 5 if member_count == 16 else None
    held = {0: ordered}
    for offset in offsets[1:]:
        held[offset] = fetch(embeddings if offset == first else ordered, offset)
    if first is not None:
        spot = jnp.array([ring.index(m) for m in range(member_count)], jnp.int32)[position]
        sender = jnp.array(ring, jnp.int32)[(spot + first) % member_count]
        sender_order = lax.dynamic_slice_in_dim(block_order[0], sender * per_device, per_device)
        held[first] = jnp.take(
            held[first].reshape(per_device, BLK, width), sender_order, axis=0
        ).reshape(row_count, width)
    norms = {}
    partial = {offset: [None] * len(spans) for offset in offsets}

    def add(offset, index, value):
        slot = partial[offset]
        slot[index] = value if slot[index] is None else slot[index] + value

    def blocks(chosen):
        for offset in {o for a, b, _ in chosen for o in (a, b)} | {0}:
            if offset not in norms:
                norms[offset] = squared(held[offset])
        groups = {}
        for a, b, both in chosen:
            groups.setdefault((a, both), []).append(b)
        for index, (start, end) in enumerate(spans):
            for (a, both), others in groups.items():
                if not both:
                    for b in others:
                        rows, _ = kernel_sums(
                            held[a][start:end], held[b][start:end],
                            norms[a][start:end], norms[b][start:end], False,
                        )
                        add(a, index, rows)
                    continue
                rows, cols = kernel_sums(
                    held[a][start:end],
                    jnp.concatenate([held[b][start:end] for b in others]),
                    norms[a][start:end],
                    jnp.concatenate([norms[b][start:end] for b in others]),
                    True,
                )
                add(a, index, rows)
                for slot, b in enumerate(others):
                    add(b, index, cols[slot * (end - start):(slot + 1) * (end - start)])

    late_pairs = [p for p in pairs if late in p[:2]]
    blocks([(0, 0, False)] + [p for p in pairs if late not in p[:2]])
    partial = lax.optimization_barrier(partial)
    blocks(late_pairs)

    def joined(offset):
        parts = [
            value if value is not None else jnp.zeros((end - start,), jnp.float32)
            for value, (start, end) in zip(partial[offset], spans)
        ]
        return jnp.concatenate(parts)

    touched = {o for a, b, both in late_pairs for o in ((a, b) if both else (a,))}
    density = joined(0)
    for offset in [o for o in offsets[1:] if o not in touched]:
        density = density + give_back(joined(offset), offset)
    for offset in [o for o in offsets[1:] if o in touched]:
        density = density + give_back(joined(offset), offset)

    inverse = 1.0 / density.reshape(per_device, BLK)
    total = grand_total(jnp.sum(inverse), ("clu", "mem"), lax.axis_size("clu") * member_count)
    everything = jnp.float32(row_count * lax.axis_size("clu") * member_count)
    spots = jnp.arange(per_device, dtype=jnp.int32)
    back = jnp.sum(
        jnp.where(order[None, :] == spots[:, None], spots[None, :], 0), axis=1
    )
    stored = jnp.take(inverse, back, axis=0).reshape(-1)
    return stored * (everything / total)


def solution(mesh):
    placed = (P(("clu", "mem"), None), P("clu", None))
    return jax.shard_map(
        shards, mesh=mesh, in_specs=placed, out_specs=P(("clu", "mem")), check_vma=False
    )
```

```python
import itertools

import jax
import jax.numpy as jnp
from jax import lax
from jax.sharding import PartitionSpec as P


BLK = 128


def squared(values):
    return jnp.sum(jnp.square(values.astype(jnp.float32)), axis=1)


def class_spans(count):
    spans = []
    start = 0
    width = count // 2
    while start < count:
        end = min(start + max(width, 1), count)
        spans.append((start, end))
        start = end
        width //= 2
    return spans


def member_ring(count):
    if count != 16:
        return list(range(count))
    chips = [(0, 0), (0, 1), (0, 2), (0, 3), (1, 3), (1, 2), (1, 1), (1, 0)]
    return [x * 8 + z * 2 + core for core in (0, 1) for x, z in chips]


def cover(count):
    if count == 16:
        return (0, 1, 5, 8, 15)
    best = None
    half = count // 2
    for size in range(2, count + 1):
        for rest in itertools.combinations(range(1, count), size - 1):
            offsets = (0,) + rest
            kinds = set()
            for a, b in itertools.combinations(offsets, 2):
                step = (b - a) % count
                kinds.add(min(step, count - step))
            if kinds >= set(range(1, half + 1)):
                cost = sum(min(d, count - d) for d in rest)
                if best is None or cost < best[0]:
                    best = (cost, offsets)
        if best is not None:
            return best[1]
    return tuple(range(count))


def plan(count):
    offsets = cover(count)
    pairs = []
    for step in range(1, count // 2 + 1):
        for a, b in itertools.permutations(offsets, 2):
            if (b - a) % count == step:
                pairs.append((a, b, 2 * step != count))
                break
    return offsets, pairs


def grand_total(value, axes, size):
    spread = lax.all_to_all(jnp.broadcast_to(value, (size,)), axes, 0, 0, tiled=True)
    return jnp.sum(spread)


def kernel_sums(left, right, left_norms, right_norms, both):
    products = lax.dot_general(
        left, right, (((1,), (1,)), ((), ())), preferred_element_type=jnp.float32
    )
    distance = left_norms[:, None] + right_norms[None, :] - 2.0 * products
    kernel = jnp.exp(-0.5 * distance)
    rows = jnp.sum(kernel, axis=1)
    cols = jnp.sum(kernel, axis=0) if both else None
    return rows, cols


def shards(embeddings, block_order):
    row_count, width = embeddings.shape
    member_count = lax.axis_size("mem")
    position = lax.axis_index("mem")
    per_device = row_count // BLK
    order = lax.dynamic_slice_in_dim(block_order[0], position * per_device, per_device)
    blocks = embeddings.reshape(per_device, BLK, width)
    pick = (order[:, None] == jnp.arange(per_device, dtype=jnp.int32)[None, :]).astype(embeddings.dtype)
    ordered = jnp.einsum(
        "sl,lrd->srd", pick, blocks, preferred_element_type=jnp.float32
    ).astype(embeddings.dtype).reshape(row_count, width)
    spans = [(start * BLK, end * BLK) for start, end in class_spans(per_device)]

    ring = member_ring(member_count)
    offsets, pairs = plan(member_count)

    def fetch(value, offset):
        return lax.ppermute(
            value,
            "mem",
            [(ring[(r + offset) % member_count], ring[r]) for r in range(member_count)],
        )

    def give_back(value, offset):
        return lax.ppermute(
            value,
            "mem",
            [(ring[r], ring[(r + offset) % member_count]) for r in range(member_count)],
        )

    late = offsets[-1]
    cut = spans[0][1]
    held = {0: ordered}
    for offset in offsets[1:]:
        if offset == late:
            head = fetch(ordered[:cut], offset)
            tail = fetch(ordered[cut:], offset)
            held[offset] = jnp.concatenate([head, tail])
            late_norms = jnp.concatenate([squared(head), squared(tail)])
        else:
            held[offset] = fetch(ordered, offset)
    norms = {late: late_norms}
    partial = {offset: [None] * len(spans) for offset in offsets}

    def add(offset, index, value):
        slot = partial[offset]
        slot[index] = value if slot[index] is None else slot[index] + value

    def blocks(chosen, classes=None):
        for offset in {o for a, b, _ in chosen for o in (a, b)} | {0}:
            if offset not in norms:
                norms[offset] = squared(held[offset])
        groups = {}
        for a, b, both in chosen:
            groups.setdefault((a, both), []).append(b)
        for index, (start, end) in enumerate(spans):
            if classes is not None and index not in classes:
                continue
            for (a, both), others in groups.items():
                if not both:
                    for b in others:
                        rows, _ = kernel_sums(
                            held[a][start:end], held[b][start:end],
                            norms[a][start:end], norms[b][start:end], False,
                        )
                        add(a, index, rows)
                    continue
                rows, cols = kernel_sums(
                    held[a][start:end],
                    jnp.concatenate([held[b][start:end] for b in others]),
                    norms[a][start:end],
                    jnp.concatenate([norms[b][start:end] for b in others]),
                    True,
                )
                add(a, index, rows)
                for slot, b in enumerate(others):
                    add(b, index, cols[slot * (end - start):(slot + 1) * (end - start)])

    late_pairs = [p for p in pairs if late in p[:2]]
    blocks([(0, 0, False)] + [p for p in pairs if late not in p[:2]])
    blocks(late_pairs, {0})
    partial = lax.optimization_barrier(partial)
    blocks(late_pairs, set(range(1, len(spans))))

    def joined(offset):
        parts = [
            value if value is not None else jnp.zeros((end - start,), jnp.float32)
            for value, (start, end) in zip(partial[offset], spans)
        ]
        return jnp.concatenate(parts)

    touched = {o for a, b, both in late_pairs for o in ((a, b) if both else (a,))}
    density = joined(0)
    for offset in [o for o in offsets[1:] if o not in touched]:
        density = density + give_back(joined(offset), offset)
    for offset in [o for o in offsets[1:] if o in touched]:
        density = density + give_back(joined(offset), offset)

    inverse = 1.0 / density.reshape(per_device, BLK)
    total = grand_total(jnp.sum(inverse), ("clu", "mem"), lax.axis_size("clu") * member_count)
    everything = jnp.float32(row_count * lax.axis_size("clu") * member_count)
    spots = jnp.arange(per_device, dtype=jnp.int32)
    back = jnp.sum(
        jnp.where(order[None, :] == spots[:, None], spots[None, :], 0), axis=1
    )
    stored = inverse.at[back].get(mode="promise_in_bounds").reshape(-1)
    return stored * (everything / total)


def solution(mesh):
    placed = (P(("clu", "mem"), None), P("clu", None))
    return jax.shard_map(
        shards, mesh=mesh, in_specs=placed, out_specs=P(("clu", "mem")), check_vma=False
    )
```

```python
import itertools

import jax
import jax.numpy as jnp
from jax import lax
from jax.sharding import PartitionSpec as P


BLK = 128


def squared(values):
    return jnp.sum(jnp.square(values.astype(jnp.float32)), axis=1)


def class_spans(count):
    spans = []
    start = 0
    width = count // 2
    while start < count:
        end = min(start + max(width, 1), count)
        spans.append((start, end))
        start = end
        width //= 2
    return spans


def member_ring(count):
    if count != 16:
        return list(range(count))
    chips = [(0, 0), (0, 1), (0, 2), (0, 3), (1, 3), (1, 2), (1, 1), (1, 0)]
    return [x * 8 + z * 2 + core for core in (0, 1) for x, z in chips]


def cover(count):
    if count == 16:
        return (0, 1, 5, 8, 15)
    best = None
    half = count // 2
    for size in range(2, count + 1):
        for rest in itertools.combinations(range(1, count), size - 1):
            offsets = (0,) + rest
            kinds = set()
            for a, b in itertools.combinations(offsets, 2):
                step = (b - a) % count
                kinds.add(min(step, count - step))
            if kinds >= set(range(1, half + 1)):
                cost = sum(min(d, count - d) for d in rest)
                if best is None or cost < best[0]:
                    best = (cost, offsets)
        if best is not None:
            return best[1]
    return tuple(range(count))


def plan(count):
    offsets = cover(count)
    pairs = []
    for step in range(1, count // 2 + 1):
        for a, b in itertools.permutations(offsets, 2):
            if (b - a) % count == step:
                pairs.append((a, b, 2 * step != count))
                break
    return offsets, pairs


def grand_total(value, axes, size):
    spread = lax.all_to_all(jnp.broadcast_to(value, (size,)), axes, 0, 0, tiled=True)
    return jnp.sum(spread)


def kernel_sums(left, right, left_norms, right_norms, both):
    products = lax.dot_general(
        left, right, (((1,), (1,)), ((), ())), preferred_element_type=jnp.float32
    )
    distance = left_norms[:, None] + right_norms[None, :] - 2.0 * products
    kernel = jnp.exp(-0.5 * distance)
    rows = jnp.sum(kernel, axis=1)
    cols = jnp.sum(kernel, axis=0) if both else None
    return rows, cols


def shards(embeddings, block_order):
    row_count, width = embeddings.shape
    member_count = lax.axis_size("mem")
    position = lax.axis_index("mem")
    per_device = row_count // BLK
    order = lax.dynamic_slice_in_dim(block_order[0], position * per_device, per_device)
    blocks = embeddings.reshape(per_device, BLK, width)
    ordered = blocks.at[order].get(mode="promise_in_bounds").reshape(row_count, width)
    spans = [(start * BLK, end * BLK) for start, end in class_spans(per_device)]

    ring = member_ring(member_count)
    offsets, pairs = plan(member_count)

    def fetch(value, offset):
        return lax.ppermute(
            value,
            "mem",
            [(ring[(r + offset) % member_count], ring[r]) for r in range(member_count)],
        )

    def give_back(value, offset):
        return lax.ppermute(
            value,
            "mem",
            [(ring[r], ring[(r + offset) % member_count]) for r in range(member_count)],
        )

    late = offsets[-1]
    cut = spans[0][1]
    held = {0: ordered}
    for offset in offsets[1:]:
        if offset == late:
            head = fetch(ordered[:cut], offset)
            tail = fetch(ordered[cut:], offset)
            held[offset] = jnp.concatenate([head, tail])
            late_norms = jnp.concatenate([squared(head), squared(tail)])
        else:
            held[offset] = fetch(ordered, offset)
    norms = {late: late_norms}
    partial = {offset: [None] * len(spans) for offset in offsets}

    def add(offset, index, value):
        slot = partial[offset]
        slot[index] = value if slot[index] is None else slot[index] + value

    def blocks(chosen, classes=None):
        for offset in {o for a, b, _ in chosen for o in (a, b)} | {0}:
            if offset not in norms:
                norms[offset] = squared(held[offset])
        groups = {}
        for a, b, both in chosen:
            groups.setdefault((a, both), []).append(b)
        for index, (start, end) in enumerate(spans):
            if classes is not None and index not in classes:
                continue
            for (a, both), others in groups.items():
                if not both:
                    for b in others:
                        rows, _ = kernel_sums(
                            held[a][start:end], held[b][start:end],
                            norms[a][start:end], norms[b][start:end], False,
                        )
                        add(a, index, rows)
                    continue
                rows, cols = kernel_sums(
                    held[a][start:end],
                    jnp.concatenate([held[b][start:end] for b in others]),
                    norms[a][start:end],
                    jnp.concatenate([norms[b][start:end] for b in others]),
                    True,
                )
                add(a, index, rows)
                for slot, b in enumerate(others):
                    add(b, index, cols[slot * (end - start):(slot + 1) * (end - start)])

    late_pairs = [p for p in pairs if late in p[:2]]
    blocks([(0, 0, False)] + [p for p in pairs if late not in p[:2]])
    blocks(late_pairs, {0})
    partial = lax.optimization_barrier(partial)
    blocks(late_pairs, set(range(1, len(spans))))

    def joined(offset):
        parts = [
            value if value is not None else jnp.zeros((end - start,), jnp.float32)
            for value, (start, end) in zip(partial[offset], spans)
        ]
        return jnp.concatenate(parts)

    touched = {o for a, b, both in late_pairs for o in ((a, b) if both else (a,))}
    density = joined(0)
    for offset in [o for o in offsets[1:] if o not in touched]:
        density = density + give_back(joined(offset), offset)
    for offset in [o for o in offsets[1:] if o in touched]:
        density = density + give_back(joined(offset), offset)

    inverse = 1.0 / density.reshape(per_device, BLK)
    total = grand_total(jnp.sum(inverse), ("clu", "mem"), lax.axis_size("clu") * member_count)
    everything = jnp.float32(row_count * lax.axis_size("clu") * member_count)
    spots = jnp.arange(per_device, dtype=jnp.int32)
    back = jnp.sum(
        jnp.where(order[None, :] == spots[:, None], spots[None, :], 0), axis=1
    )
    stored = inverse.at[back].get(mode="promise_in_bounds").reshape(-1)
    return stored * (everything / total)


def solution(mesh):
    placed = (P(("clu", "mem"), None), P("clu", None))
    return jax.shard_map(
        shards, mesh=mesh, in_specs=placed, out_specs=P(("clu", "mem")), check_vma=False
    )
```

```python
import itertools

import jax
import jax.numpy as jnp
from jax import lax
from jax.sharding import PartitionSpec as P


BLK = 128


def squared(values):
    return jnp.sum(jnp.square(values.astype(jnp.float32)), axis=1)


def class_spans(count):
    spans = []
    start = 0
    width = count // 2
    while start < count:
        end = min(start + max(width, 1), count)
        spans.append((start, end))
        start = end
        width //= 2
    return spans


def member_ring(count):
    if count != 16:
        return list(range(count))
    chips = [(0, 0), (0, 1), (0, 2), (0, 3), (1, 3), (1, 2), (1, 1), (1, 0)]
    return [x * 8 + z * 2 + core for core in (0, 1) for x, z in chips]


def cover(count):
    if count == 16:
        return (0, 1, 5, 8, 15)
    best = None
    half = count // 2
    for size in range(2, count + 1):
        for rest in itertools.combinations(range(1, count), size - 1):
            offsets = (0,) + rest
            kinds = set()
            for a, b in itertools.combinations(offsets, 2):
                step = (b - a) % count
                kinds.add(min(step, count - step))
            if kinds >= set(range(1, half + 1)):
                cost = sum(min(d, count - d) for d in rest)
                if best is None or cost < best[0]:
                    best = (cost, offsets)
        if best is not None:
            return best[1]
    return tuple(range(count))


def plan(count):
    offsets = cover(count)
    pairs = []
    for step in range(1, count // 2 + 1):
        for a, b in itertools.permutations(offsets, 2):
            if (b - a) % count == step:
                pairs.append((a, b, 2 * step != count))
                break
    return offsets, pairs


def grand_total(value, axes, size):
    spread = lax.all_to_all(jnp.broadcast_to(value, (size,)), axes, 0, 0, tiled=True)
    return jnp.sum(spread)


def kernel_sums(left, right, left_norms, right_norms, both):
    products = lax.dot_general(
        left, right, (((1,), (1,)), ((), ())), preferred_element_type=jnp.float32
    )
    distance = left_norms[:, None] + right_norms[None, :] - 2.0 * products
    kernel = jnp.exp(-0.5 * distance)
    rows = jnp.sum(kernel, axis=1)
    cols = jnp.sum(kernel, axis=0) if both else None
    return rows, cols


def shards(embeddings, block_order):
    row_count, width = embeddings.shape
    member_count = lax.axis_size("mem")
    position = lax.axis_index("mem")
    per_device = row_count // BLK
    order = lax.dynamic_slice_in_dim(block_order[0], position * per_device, per_device)
    blocks = embeddings.reshape(per_device, BLK, width)
    ordered = blocks.at[order].get(mode="promise_in_bounds").reshape(row_count, width)
    spans = [(start * BLK, end * BLK) for start, end in class_spans(per_device)]

    ring = member_ring(member_count)
    offsets, pairs = plan(member_count)

    def fetch(value, offset):
        return lax.ppermute(
            value,
            "mem",
            [(ring[(r + offset) % member_count], ring[r]) for r in range(member_count)],
        )

    def give_back(value, offset):
        return lax.ppermute(
            value,
            "mem",
            [(ring[r], ring[(r + offset) % member_count]) for r in range(member_count)],
        )

    late = offsets[-1]
    cut = spans[1][1]
    held = {0: ordered}
    for offset in offsets[1:]:
        if offset == late:
            head = fetch(ordered[:cut], offset)
            tail = fetch(ordered[cut:], offset)
            held[offset] = jnp.concatenate([head, tail])
            late_norms = jnp.concatenate([squared(head), squared(tail)])
        else:
            held[offset] = fetch(ordered, offset)
    norms = {late: late_norms}
    partial = {offset: [None] * len(spans) for offset in offsets}

    def add(offset, index, value):
        slot = partial[offset]
        slot[index] = value if slot[index] is None else slot[index] + value

    def blocks(chosen, classes=None):
        for offset in {o for a, b, _ in chosen for o in (a, b)} | {0}:
            if offset not in norms:
                norms[offset] = squared(held[offset])
        groups = {}
        for a, b, both in chosen:
            groups.setdefault((a, both), []).append(b)
        for index, (start, end) in enumerate(spans):
            if classes is not None and index not in classes:
                continue
            for (a, both), others in groups.items():
                if not both:
                    for b in others:
                        rows, _ = kernel_sums(
                            held[a][start:end], held[b][start:end],
                            norms[a][start:end], norms[b][start:end], False,
                        )
                        add(a, index, rows)
                    continue
                rows, cols = kernel_sums(
                    held[a][start:end],
                    jnp.concatenate([held[b][start:end] for b in others]),
                    norms[a][start:end],
                    jnp.concatenate([norms[b][start:end] for b in others]),
                    True,
                )
                add(a, index, rows)
                for slot, b in enumerate(others):
                    add(b, index, cols[slot * (end - start):(slot + 1) * (end - start)])

    late_pairs = [p for p in pairs if late in p[:2]]
    blocks([(0, 0, False)] + [p for p in pairs if late not in p[:2]])
    blocks(late_pairs, {0, 1})
    partial = lax.optimization_barrier(partial)
    blocks(late_pairs, set(range(2, len(spans))))

    def joined(offset):
        parts = [
            value if value is not None else jnp.zeros((end - start,), jnp.float32)
            for value, (start, end) in zip(partial[offset], spans)
        ]
        return jnp.concatenate(parts)

    touched = {o for a, b, both in late_pairs for o in ((a, b) if both else (a,))}
    density = joined(0)
    for offset in [o for o in offsets[1:] if o not in touched]:
        density = density + give_back(joined(offset), offset)
    for offset in [o for o in offsets[1:] if o in touched]:
        density = density + give_back(joined(offset), offset)

    inverse = 1.0 / density.reshape(per_device, BLK)
    total = grand_total(jnp.sum(inverse), ("clu", "mem"), lax.axis_size("clu") * member_count)
    everything = jnp.float32(row_count * lax.axis_size("clu") * member_count)
    spots = jnp.arange(per_device, dtype=jnp.int32)
    back = jnp.sum(
        jnp.where(order[None, :] == spots[:, None], spots[None, :], 0), axis=1
    )
    stored = inverse.at[back].get(mode="promise_in_bounds").reshape(-1)
    return stored * (everything / total)


def solution(mesh):
    placed = (P(("clu", "mem"), None), P("clu", None))
    return jax.shard_map(
        shards, mesh=mesh, in_specs=placed, out_specs=P(("clu", "mem")), check_vma=False
    )
```
